768 devices in a mesh: dp: 64 (over y, z_hi, core), block: 12 (over z_lo, x).
Axes of the slice: x: 4, y: 8, z: 12 (z_hi: 4, z_lo: 3; z = z_hi * 3 + z_lo), core: 2. Of those that a mesh axis runs over, the one named last changes fastest.
Arguments:
- tokens: bfloat16 [18432, 6144], P('dp', 'block'), may hold values from -6 to 6
- up_first: bfloat16 [96, 64, 256], P('block'), may hold values from -0.75 to 0.75
- up_mix: bfloat16 [256, 96, 96], replicated, may hold values from -0.625 to 0.625
- down_mix: bfloat16 [256, 96, 96], replicated, may hold values from -0.625 to 0.625
- down_last: bfloat16 [96, 64, 256], P('block'), may hold values from -0.375 to 0.375
- cotangent: bfloat16 [18432, 6144], P('dp', 'block'), may hold values from -6 to 6
Outputs:
- encoded: bfloat16 [18432, 6144], P('dp', 'block')
- grad_tokens: bfloat16 [18432, 6144], P('dp', 'block')
- grad_up_first: float32 [96, 64, 256], P('block')
- grad_down_last: float32 [96, 64, 256], P('block')
The draws below stay inside these ranges and needn't reach their ends.
All inputs are finite; a program needn't handle non-finite values.
Results may differ from the reference program's by a relative error of at most 0.014.
Values may be sent and summed in bfloat16 or wider, within the bound.
No kernel may reach another device: no remote copies, remote signals or barrier semaphores. Data moves between devices by JAX's collectives and lax.ppermute only.
A program may use at most 64 MiB of HBM per device.

```python
import jax
import jax.numpy as jnp
from jax import lax

D = 6144
NB = 96
BIN = 64
BH = 256
TOK_DEV = 288
TOKENS = 18432
N_DP = 64


def block_levels(own_key, extent, cuts, smallest, largest):
    factor_of, own = 1.0, jax.random.fold_in(own_key, 6)
    for dim, blocks in cuts:
        steps = jnp.exp(jax.random.uniform(jax.random.fold_in(own, dim), (blocks,), jnp.float32, smallest / len(cuts), largest / len(cuts)))
        factor_of = factor_of * jnp.repeat(steps, extent[dim] // blocks).reshape([-1 if axis == dim else 1 for axis in range(len(extent))])
    return factor_of


def normal_values(key, dims, spread, limit, split=(), kind=jnp.bfloat16):
    values = spread * jax.random.normal(key, dims, jnp.float32)
    if split:
        values = values * block_levels(key, dims, split, -0.22, 0.18)
    return jnp.clip(values, -limit, limit).astype(kind)


def setup_inputs(seed: int = 0) -> dict:
    seeds = jax.random.split(jax.random.key(seed), 7)
    tokens = normal_values(seeds[0], (TOKENS, D), 1.0, 6.0, ((0, 64), (1, 12)))
    up_first = normal_values(seeds[1], (NB, BIN, BH), BIN ** -0.5, 0.75, ((0, 12),))
    up_mix = normal_values(seeds[2], (BH, NB, NB), NB ** -0.5, 0.625)
    down_mix = normal_values(seeds[3], (BH, NB, NB), NB ** -0.5, 0.625)
    down_last = normal_values(seeds[4], (NB, BIN, BH), BH ** -0.5, 0.375, ((0, 12),))
    cotangent = normal_values(seeds[5], (TOKENS, D), 1.0, 6.0, ((0, 64), (1, 12)))
    return dict(tokens=tokens, up_first=up_first, up_mix=up_mix, down_mix=down_mix, down_last=down_last, cotangent=cotangent)


gelu_coef = 0.7978845608028654
cubic_coef = 0.044715


def gelu_pair(values):
    inner = gelu_coef * (values + cubic_coef * values * values * values)
    tangent = jnp.tanh(inner)
    result = 0.5 * values * (1.0 + tangent)
    slope = 0.5 * (1.0 + tangent) + 0.5 * values * (1.0 - tangent * tangent) * gelu_coef * (1.0 + 3.0 * cubic_coef * values * values)
    return result, slope


def reference(tokens, up_first, up_mix, down_mix, down_last, cotangent):
    flt = jnp.float32
    half = jnp.bfloat16
    inputs = tokens.reshape(N_DP, TOK_DEV, NB, BIN)
    outgrads = cotangent.reshape(N_DP, TOK_DEV, NB, BIN)
    first_w = up_first.astype(flt)
    upmix_w = up_mix.astype(flt)
    downmix_w = down_mix.astype(flt)
    last_w = down_last.astype(flt)

    def one_block(totals, pieces):
        inblock, gblock = pieces
        inblock = inblock.astype(flt)
        gblock = gblock.astype(flt)
        first = jnp.einsum('trk,rkc->trc', inblock, first_w).astype(half)
        preact = jnp.einsum('trc,csr->tsc', first.astype(flt), upmix_w).astype(half)
        hidden_f, slope = gelu_pair(preact.astype(flt))
        hidden = hidden_f.astype(half)
        mixed = jnp.einsum('tsc,cqs->tqc', hidden.astype(flt), downmix_w).astype(half)
        encoded = jnp.einsum('tqc,qkc->tqk', mixed.astype(flt), last_w).astype(half)
        grad_mixed = jnp.einsum('tqk,qkc->tqc', gblock, last_w).astype(half)
        grad_last = jnp.einsum('tqk,tqc->qkc', gblock, mixed.astype(flt))
        grad_hidden = jnp.einsum('tqc,cqs->tsc', grad_mixed.astype(flt), downmix_w).astype(half)
        grad_pre = (grad_hidden.astype(flt) * slope).astype(half)
        grad_first = jnp.einsum('tsc,csr->trc', grad_pre.astype(flt), upmix_w).astype(half)
        grad_in = jnp.einsum('trc,rkc->trk', grad_first.astype(flt), first_w).astype(half)
        grad_firstw = jnp.einsum('trk,trc->rkc', inblock, grad_first.astype(flt))
        return (totals[0] + grad_firstw, totals[1] + grad_last), (encoded, grad_in)

    zeros = (jnp.zeros((NB, BIN, BH), flt), jnp.zeros((NB, BIN, BH), flt))
    totals, outputs = lax.scan(one_block, zeros, (inputs, outgrads))
    encoded = outputs[0].reshape(TOKENS, D)
    grad_tokens = outputs[1].reshape(TOKENS, D)
    return (encoded, grad_tokens, totals[0], totals[1])
```

```python
import jax
import jax.numpy as jnp
from jax import lax
from jax.sharding import PartitionSpec as P, Mesh
DP = ("y", "zh", "core")
BLK = ("zl", "x")

gelu_coef = 0.7978845608028654
cubic_coef = 0.044715


def gelu_pair(values):
    inner = gelu_coef * (values + cubic_coef * values * values * values)
    tangent = jnp.tanh(inner)
    result = 0.5 * values * (1.0 + tangent)
    slope = 0.5 * (1.0 + tangent) + 0.5 * values * (1.0 - tangent * tangent) * gelu_coef * (
        1.0 + 3.0 * cubic_coef * values * values
    )
    return (result, slope)


def to_tokens(panel):
    return lax.all_to_all(panel, BLK, split_axis=0, concat_axis=1, tiled=True)


def to_blocks(panel):
    return lax.all_to_all(panel, BLK, split_axis=1, concat_axis=0, tiled=True)


def shards(tokens, up_first, up_mix, down_mix, down_last, cotangent):
    flt = jnp.float32
    half = jnp.bfloat16
    row_count = tokens.shape[0]
    local_blocks = up_first.shape[0]
    width_in = up_first.shape[1]
    inputs = tokens.reshape(row_count, local_blocks, width_in)
    outgrads = cotangent.reshape(row_count, local_blocks, width_in)
    first = jnp.einsum("trk,rkc->trc", inputs, up_first, preferred_element_type=flt).astype(half)
    grad_mixed = jnp.einsum("tqk,qkc->tqc", outgrads, down_last, preferred_element_type=flt).astype(
        half
    )
    first_tok = to_tokens(first)
    pre_tok = jnp.einsum("trc,csr->tsc", first_tok, up_mix, preferred_element_type=flt).astype(half)
    hidden_f, slope = gelu_pair(pre_tok.astype(flt))
    hidden_tok = hidden_f.astype(half)
    mixed_tok = jnp.einsum("tsc,cqs->tqc", hidden_tok, down_mix, preferred_element_type=flt).astype(
        half
    )
    mixed = to_blocks(mixed_tok)
    encoded = jnp.einsum("tqc,qkc->tqk", mixed, down_last, preferred_element_type=flt).astype(half)
    grad_last = jnp.einsum("tqk,tqc->qkc", outgrads, mixed, preferred_element_type=flt)
    grad_mixed_tok = to_tokens(grad_mixed)
    grad_hidden_tok = jnp.einsum(
        "tqc,cqs->tsc", grad_mixed_tok, down_mix, preferred_element_type=flt
    ).astype(half)
    grad_pre_tok = (grad_hidden_tok.astype(flt) * slope).astype(half)
    grad_first_tok = jnp.einsum(
        "tsc,csr->trc", grad_pre_tok, up_mix, preferred_element_type=flt
    ).astype(half)
    grad_first = to_blocks(grad_first_tok)
    grad_in = jnp.einsum("trc,rkc->trk", grad_first, up_first, preferred_element_type=flt).astype(
        half
    )
    grad_firstw = jnp.einsum("trk,trc->rkc", inputs, grad_first, preferred_element_type=flt)

    both = jnp.concatenate([grad_firstw.reshape(-1, grad_firstw.shape[-1]), grad_last.reshape(-1, grad_last.shape[-1])], axis=0)
    both = lax.psum_scatter(both, DP, scatter_dimension=0, tiled=True)
    both = lax.all_gather(both, DP, axis=0, tiled=True)
    summed_first, summed_last = jnp.split(both, 2, axis=0)
    summed_first = summed_first.reshape(grad_firstw.shape)
    summed_last = summed_last.reshape(grad_last.shape)
    return (
        encoded.reshape(row_count, local_blocks * width_in),
        grad_in.reshape(row_count, local_blocks * width_in),
        summed_first,
        summed_last,
    )


def solution(mesh):
    mesh = Mesh(mesh.devices.reshape(8, 4, 2, 3, 4), ("y", "zh", "core", "zl", "x"))
    placed = (
        P(DP, BLK),
        P(BLK, None, None),
        P(),
        P(),
        P(BLK, None, None),
        P(DP, BLK),
    )
    return jax.shard_map(
        shards,
        mesh=mesh,
        in_specs=placed,
        out_specs=(
            P(DP, BLK),
            P(DP, BLK),
            P(BLK, None, None),
            P(BLK, None, None),
        ),
        check_vma=False,
    )
```

```python
import jax
import jax.numpy as jnp
from jax import lax
from jax.sharding import PartitionSpec as P, Mesh
DP = ("y", "zh", "core")
BLK = ("zl", "x")

gelu_coef = 0.7978845608028654
cubic_coef = 0.044715


def gelu_pair(values):
    inner = gelu_coef * (values + cubic_coef * values * values * values)
    tangent = jnp.tanh(inner)
    result = 0.5 * values * (1.0 + tangent)
    slope = 0.5 * (1.0 + tangent) + 0.5 * values * (1.0 - tangent * tangent) * gelu_coef * (
        1.0 + 3.0 * cubic_coef * values * values
    )
    return (result, slope)


def to_tokens(panel):
    return lax.all_to_all(panel, BLK, split_axis=0, concat_axis=1, tiled=True)


def to_blocks(panel):
    return lax.all_to_all(panel, BLK, split_axis=1, concat_axis=0, tiled=True)


def shards(tokens, up_first, up_mix, down_mix, down_last, cotangent):
    flt = jnp.float32
    half = jnp.bfloat16
    row_count = tokens.shape[0]
    local_blocks = up_first.shape[0]
    width_in = up_first.shape[1]
    inputs = tokens.reshape(row_count, local_blocks, width_in)
    outgrads = cotangent.reshape(row_count, local_blocks, width_in)
    first = jnp.einsum("trk,rkc->trc", inputs, up_first, preferred_element_type=flt).astype(half)
    grad_mixed = jnp.einsum("tqk,qkc->tqc", outgrads, down_last, preferred_element_type=flt).astype(
        half
    )
    first_tok = to_tokens(first)
    pre_tok = jnp.einsum("trc,csr->tsc", first_tok, up_mix, preferred_element_type=flt).astype(half)
    hidden_f, slope = gelu_pair(pre_tok.astype(flt))
    hidden_tok = hidden_f.astype(half)
    mixed_tok = jnp.einsum("tsc,cqs->tqc", hidden_tok, down_mix, preferred_element_type=flt).astype(
        half
    )
    mixed = to_blocks(mixed_tok)
    encoded = jnp.einsum("tqc,qkc->tqk", mixed, down_last, preferred_element_type=flt).astype(half)
    grad_last = jnp.einsum("tqk,tqc->qkc", outgrads, mixed, preferred_element_type=flt)
    grad_mixed_tok = to_tokens(grad_mixed)
    grad_hidden_tok = jnp.einsum(
        "tqc,cqs->tsc", grad_mixed_tok, down_mix, preferred_element_type=flt
    ).astype(half)
    grad_pre_tok = (grad_hidden_tok.astype(flt) * slope).astype(half)
    grad_first_tok = jnp.einsum(
        "tsc,csr->trc", grad_pre_tok, up_mix, preferred_element_type=flt
    ).astype(half)
    grad_first = to_blocks(grad_first_tok)
    grad_in = jnp.einsum("trc,rkc->trk", grad_first, up_first, preferred_element_type=flt).astype(
        half
    )
    grad_firstw = jnp.einsum("trk,trc->rkc", inputs, grad_first, preferred_element_type=flt)

    both = jnp.concatenate([grad_firstw.reshape(-1, grad_firstw.shape[-1]), grad_last.reshape(-1, grad_last.shape[-1])], axis=0)
    parts = lax.all_to_all(both.reshape(64, -1, both.shape[-1]), DP, 0, 0, tiled=True)
    part = parts.sum(axis=0)
    spread = jnp.broadcast_to(part[None], (64,) + part.shape)
    both = lax.all_to_all(spread, DP, 0, 0, tiled=True).reshape(-1, part.shape[-1])
    summed_first, summed_last = jnp.split(both, 2, axis=0)
    summed_first = summed_first.reshape(grad_firstw.shape)
    summed_last = summed_last.reshape(grad_last.shape)
    return (
        encoded.reshape(row_count, local_blocks * width_in),
        grad_in.reshape(row_count, local_blocks * width_in),
        summed_first,
        summed_last,
    )


def solution(mesh):
    mesh = Mesh(mesh.devices.reshape(8, 4, 2, 3, 4), ("y", "zh", "core", "zl", "x"))
    placed = (
        P(DP, BLK),
        P(BLK, None, None),
        P(),
        P(),
        P(BLK, None, None),
        P(DP, BLK),
    )
    return jax.shard_map(
        shards,
        mesh=mesh,
        in_specs=placed,
        out_specs=(
            P(DP, BLK),
            P(DP, BLK),
            P(BLK, None, None),
            P(BLK, None, None),
        ),
        check_vma=False,
    )
```

```python
import jax
import jax.numpy as jnp
from jax import lax
from jax.sharding import PartitionSpec as P, Mesh
DP = ("y", "zh", "core")
BLK = ("zl", "x")
DP_ORDER = ("core", "y", "zh")

gelu_coef = 0.7978845608028654
cubic_coef = 0.044715


def gelu_pair(values):
    inner = gelu_coef * (values + cubic_coef * values * values * values)
    tangent = jnp.tanh(inner)
    result = 0.5 * values * (1.0 + tangent)
    slope = 0.5 * (1.0 + tangent) + 0.5 * values * (1.0 - tangent * tangent) * gelu_coef * (
        1.0 + 3.0 * cubic_coef * values * values
    )
    return (result, slope)


def to_tokens(panel):
    return lax.all_to_all(panel, BLK, split_axis=0, concat_axis=1, tiled=True)


def to_blocks(panel):
    return lax.all_to_all(panel, BLK, split_axis=1, concat_axis=0, tiled=True)


def dp_sum(total, sizes):
    lanes = total.shape[-1]
    for axis in DP_ORDER:
        count = sizes[axis]
        pieces = lax.all_to_all(total.reshape(count, -1, lanes), axis, 0, 0, tiled=True)
        total = pieces.sum(axis=0)
    for axis in reversed(DP_ORDER):
        count = sizes[axis]
        spread = jnp.broadcast_to(total[None], (count,) + total.shape)
        total = lax.all_to_all(spread, axis, 0, 0, tiled=True).reshape(-1, lanes)
    return total


def shards(tokens, up_first, up_mix, down_mix, down_last, cotangent):
    mesh_sizes = {"core": 2, "y": 8, "zh": 4}
    flt = jnp.float32
    half = jnp.bfloat16
    row_count = tokens.shape[0]
    local_blocks = up_first.shape[0]
    width_in = up_first.shape[1]
    inputs = tokens.reshape(row_count, local_blocks, width_in)
    outgrads = cotangent.reshape(row_count, local_blocks, width_in)
    first = jnp.einsum("trk,rkc->trc", inputs, up_first, preferred_element_type=flt).astype(half)
    grad_mixed = jnp.einsum("tqk,qkc->tqc", outgrads, down_last, preferred_element_type=flt).astype(
        half
    )
    first_tok = to_tokens(first)
    pre_tok = jnp.einsum("trc,csr->tsc", first_tok, up_mix, preferred_element_type=flt).astype(half)
    hidden_f, slope = gelu_pair(pre_tok.astype(flt))
    hidden_tok = hidden_f.astype(half)
    mixed_tok = jnp.einsum("tsc,cqs->tqc", hidden_tok, down_mix, preferred_element_type=flt).astype(
        half
    )
    mixed = to_blocks(mixed_tok)
    encoded = jnp.einsum("tqc,qkc->tqk", mixed, down_last, preferred_element_type=flt).astype(half)
    grad_last = jnp.einsum("tqk,tqc->qkc", outgrads, mixed, preferred_element_type=flt)
    grad_mixed_tok = to_tokens(grad_mixed)
    grad_hidden_tok = jnp.einsum(
        "tqc,cqs->tsc", grad_mixed_tok, down_mix, preferred_element_type=flt
    ).astype(half)
    grad_pre_tok = (grad_hidden_tok.astype(flt) * slope).astype(half)
    grad_first_tok = jnp.einsum(
        "tsc,csr->trc", grad_pre_tok, up_mix, preferred_element_type=flt
    ).astype(half)
    grad_first = to_blocks(grad_first_tok)
    grad_in = jnp.einsum("trc,rkc->trk", grad_first, up_first, preferred_element_type=flt).astype(
        half
    )
    grad_firstw = jnp.einsum("trk,trc->rkc", inputs, grad_first, preferred_element_type=flt)

    both = jnp.concatenate([grad_firstw.reshape(-1, grad_firstw.shape[-1]), grad_last.reshape(-1, grad_last.shape[-1])], axis=0)
    both = dp_sum(both, mesh_sizes)
    summed_first, summed_last = jnp.split(both, 2, axis=0)
    summed_first = summed_first.reshape(grad_firstw.shape)
    summed_last = summed_last.reshape(grad_last.shape)
    return (
        encoded.reshape(row_count, local_blocks * width_in),
        grad_in.reshape(row_count, local_blocks * width_in),
        summed_first,
        summed_last,
    )


def solution(mesh):
    mesh = Mesh(mesh.devices.reshape(8, 4, 2, 3, 4), ("y", "zh", "core", "zl", "x"))
    placed = (
        P(DP, BLK),
        P(BLK, None, None),
        P(),
        P(),
        P(BLK, None, None),
        P(DP, BLK),
    )
    return jax.shard_map(
        shards,
        mesh=mesh,
        in_specs=placed,
        out_specs=(
            P(DP, BLK),
            P(DP, BLK),
            P(BLK, None, None),
            P(BLK, None, None),
        ),
        check_vma=False,
    )
```

```python
import jax
import jax.numpy as jnp
from jax import lax
from jax.sharding import PartitionSpec as P, Mesh
DP = ("y", "zh", "core")
BLK = ("zl", "x")
DP_ORDER = ("core", "y", "zh")

gelu_coef = 0.7978845608028654
cubic_coef = 0.044715


def gelu_pair(values):
    inner = gelu_coef * (values + cubic_coef * values * values * values)
    tangent = jnp.tanh(inner)
    result = 0.5 * values * (1.0 + tangent)
    slope = 0.5 * (1.0 + tangent) + 0.5 * values * (1.0 - tangent * tangent) * gelu_coef * (
        1.0 + 3.0 * cubic_coef * values * values
    )
    return (result, slope)


def to_tokens(panel):
    return lax.all_to_all(panel, BLK, split_axis=1, concat_axis=2, tiled=True)


def to_blocks(panel):
    return lax.all_to_all(panel, BLK, split_axis=2, concat_axis=1, tiled=True)


def dp_sum(total, sizes):
    lanes = total.shape[-1]
    for axis in DP_ORDER:
        count = sizes[axis]
        pieces = lax.all_to_all(total.reshape(count, -1, lanes), axis, 0, 0, tiled=True)
        total = pieces.sum(axis=0)
    for axis in reversed(DP_ORDER):
        count = sizes[axis]
        spread = jnp.broadcast_to(total[None], (count,) + total.shape)
        total = lax.all_to_all(spread, axis, 0, 0, tiled=True).reshape(-1, lanes)
    return total


def shards(tokens, up_first, up_mix, down_mix, down_last, cotangent):
    mesh_sizes = {"core": 2, "y": 8, "zh": 4}
    flt = jnp.float32
    half = jnp.bfloat16
    row_count = tokens.shape[0]
    local_blocks = up_first.shape[0]
    width_in = up_first.shape[1]
    inputs = tokens.reshape(row_count, local_blocks, width_in)
    outgrads = cotangent.reshape(row_count, local_blocks, width_in)
    first = jnp.einsum("trk,rkc->trc", inputs, up_first, preferred_element_type=flt).astype(half)
    grad_mixed = jnp.einsum("tqk,qkc->tqc", outgrads, down_last, preferred_element_type=flt).astype(
        half
    )
    first_tok, grad_mixed_tok = to_tokens(jnp.stack([first, grad_mixed]))
    pre_tok = jnp.einsum("trc,csr->tsc", first_tok, up_mix, preferred_element_type=flt).astype(half)
    hidden_f, slope = gelu_pair(pre_tok.astype(flt))
    hidden_tok = hidden_f.astype(half)
    mixed_tok = jnp.einsum("tsc,cqs->tqc", hidden_tok, down_mix, preferred_element_type=flt).astype(
        half
    )
    grad_hidden_tok = jnp.einsum(
        "tqc,cqs->tsc", grad_mixed_tok, down_mix, preferred_element_type=flt
    ).astype(half)
    grad_pre_tok = (grad_hidden_tok.astype(flt) * slope).astype(half)
    grad_first_tok = jnp.einsum(
        "tsc,csr->trc", grad_pre_tok, up_mix, preferred_element_type=flt
    ).astype(half)
    mixed, grad_first = to_blocks(jnp.stack([mixed_tok, grad_first_tok]))
    encoded = jnp.einsum("tqc,qkc->tqk", mixed, down_last, preferred_element_type=flt).astype(half)
    grad_last = jnp.einsum("tqk,tqc->qkc", outgrads, mixed, preferred_element_type=flt)
    grad_in = jnp.einsum("trc,rkc->trk", grad_first, up_first, preferred_element_type=flt).astype(
        half
    )
    grad_firstw = jnp.einsum("trk,trc->rkc", inputs, grad_first, preferred_element_type=flt)

    both = jnp.concatenate([grad_firstw.reshape(-1, grad_firstw.shape[-1]), grad_last.reshape(-1, grad_last.shape[-1])], axis=0)
    both = dp_sum(both, mesh_sizes)
    summed_first, summed_last = jnp.split(both, 2, axis=0)
    summed_first = summed_first.reshape(grad_firstw.shape)
    summed_last = summed_last.reshape(grad_last.shape)
    return (
        encoded.reshape(row_count, local_blocks * width_in),
        grad_in.reshape(row_count, local_blocks * width_in),
        summed_first,
        summed_last,
    )


def solution(mesh):
    mesh = Mesh(mesh.devices.reshape(8, 4, 2, 3, 4), ("y", "zh", "core", "zl", "x"))
    placed = (
        P(DP, BLK),
        P(BLK, None, None),
        P(),
        P(),
        P(BLK, None, None),
        P(DP, BLK),
    )
    return jax.shard_map(
        shards,
        mesh=mesh,
        in_specs=placed,
        out_specs=(
            P(DP, BLK),
            P(DP, BLK),
            P(BLK, None, None),
            P(BLK, None, None),
        ),
        check_vma=False,
    )
```

```python
import jax
import jax.numpy as jnp
from jax import lax
from jax.sharding import PartitionSpec as P, Mesh
DP = ("y", "zh", "core")
BLK = ("zl", "x")
DP_ORDER = ("core", "y", "zh")

gelu_coef = 0.7978845608028654
cubic_coef = 0.044715


def gelu_pair(values):
    inner = gelu_coef * (values + cubic_coef * values * values * values)
    tangent = jnp.tanh(inner)
    result = 0.5 * values * (1.0 + tangent)
    slope = 0.5 * (1.0 + tangent) + 0.5 * values * (1.0 - tangent * tangent) * gelu_coef * (
        1.0 + 3.0 * cubic_coef * values * values
    )
    return (result, slope)


def to_tokens(panel):
    return lax.all_to_all(panel, BLK, split_axis=0, concat_axis=1, tiled=True)


def to_blocks(panel):
    return lax.all_to_all(panel, BLK, split_axis=1, concat_axis=0, tiled=True)


def ring_scatter(total, axis, count):
    me = lax.axis_index(axis)
    pieces = total.reshape(count, -1, total.shape[-1])
    acc = lax.dynamic_index_in_dim(pieces, me, keepdims=False)
    for shift in range(1, count):
        pairs = [(i, (i + shift) % count) for i in range(count)]
        sent = lax.dynamic_index_in_dim(pieces, (me + shift) % count, keepdims=False)
        acc = acc + lax.ppermute(sent, axis, pairs)
    return acc


def ring_gather(part, axis, count):
    me = lax.axis_index(axis)
    whole = jnp.zeros((count,) + part.shape, part.dtype)
    whole = lax.dynamic_update_index_in_dim(whole, part, me, 0)
    for shift in range(1, count):
        pairs = [(i, (i + shift) % count) for i in range(count)]
        got = lax.ppermute(part, axis, pairs)
        whole = lax.dynamic_update_index_in_dim(whole, got, (me - shift) % count, 0)
    return whole.reshape(-1, part.shape[-1])


def dp_sum(total, sizes):
    for axis in DP_ORDER:
        total = ring_scatter(total, axis, sizes[axis])
    for axis in reversed(DP_ORDER):
        total = ring_gather(total, axis, sizes[axis])
    return total


def shards(tokens, up_first, up_mix, down_mix, down_last, cotangent):
    mesh_sizes = {"core": 2, "y": 8, "zh": 4}
    flt = jnp.float32
    half = jnp.bfloat16
    row_count = tokens.shape[0]
    local_blocks = up_first.shape[0]
    width_in = up_first.shape[1]
    inputs = tokens.reshape(row_count, local_blocks, width_in)
    outgrads = cotangent.reshape(row_count, local_blocks, width_in)
    first = jnp.einsum("trk,rkc->trc", inputs, up_first, preferred_element_type=flt).astype(half)
    grad_mixed = jnp.einsum("tqk,qkc->tqc", outgrads, down_last, preferred_element_type=flt).astype(
        half
    )
    first_tok = to_tokens(first)
    pre_tok = jnp.einsum("trc,csr->tsc", first_tok, up_mix, preferred_element_type=flt).astype(half)
    hidden_f, slope = gelu_pair(pre_tok.astype(flt))
    hidden_tok = hidden_f.astype(half)
    mixed_tok = jnp.einsum("tsc,cqs->tqc", hidden_tok, down_mix, preferred_element_type=flt).astype(
        half
    )
    mixed = to_blocks(mixed_tok)
    encoded = jnp.einsum("tqc,qkc->tqk", mixed, down_last, preferred_element_type=flt).astype(half)
    grad_last = jnp.einsum("tqk,tqc->qkc", outgrads, mixed, preferred_element_type=flt)
    grad_mixed_tok = to_tokens(grad_mixed)
    grad_hidden_tok = jnp.einsum(
        "tqc,cqs->tsc", grad_mixed_tok, down_mix, preferred_element_type=flt
    ).astype(half)
    grad_pre_tok = (grad_hidden_tok.astype(flt) * slope).astype(half)
    grad_first_tok = jnp.einsum(
        "tsc,csr->trc", grad_pre_tok, up_mix, preferred_element_type=flt
    ).astype(half)
    grad_first = to_blocks(grad_first_tok)
    grad_in = jnp.einsum("trc,rkc->trk", grad_first, up_first, preferred_element_type=flt).astype(
        half
    )
    grad_firstw = jnp.einsum("trk,trc->rkc", inputs, grad_first, preferred_element_type=flt)

    summed_first = dp_sum(grad_firstw.reshape(-1, grad_firstw.shape[-1]), mesh_sizes)
    summed_last = dp_sum(grad_last.reshape(-1, grad_last.shape[-1]), mesh_sizes)
    summed_first = summed_first.reshape(grad_firstw.shape)
    summed_last = summed_last.reshape(grad_last.shape)
    return (
        encoded.reshape(row_count, local_blocks * width_in),
        grad_in.reshape(row_count, local_blocks * width_in),
        summed_first,
        summed_last,
    )


def solution(mesh):
    mesh = Mesh(mesh.devices.reshape(8, 4, 2, 3, 4), ("y", "zh", "core", "zl", "x"))
    placed = (
        P(DP, BLK),
        P(BLK, None, None),
        P(),
        P(),
        P(BLK, None, None),
        P(DP, BLK),
    )
    return jax.shard_map(
        shards,
        mesh=mesh,
        in_specs=placed,
        out_specs=(
            P(DP, BLK),
            P(DP, BLK),
            P(BLK, None, None),
            P(BLK, None, None),
        ),
        check_vma=False,
    )
```

```python
import jax
import jax.numpy as jnp
from jax import lax
from jax.sharding import PartitionSpec as P, Mesh
DP = ("y", "zh", "core")
BLK = ("zl", "x")
DP_ORDER = ("core", "y", "zh")

gelu_coef = 0.7978845608028654
cubic_coef = 0.044715


def gelu_pair(values):
    inner = gelu_coef * (values + cubic_coef * values * values * values)
    tangent = jnp.tanh(inner)
    result = 0.5 * values * (1.0 + tangent)
    slope = 0.5 * (1.0 + tangent) + 0.5 * values * (1.0 - tangent * tangent) * gelu_coef * (
        1.0 + 3.0 * cubic_coef * values * values
    )
    return (result, slope)


def to_tokens(panel):
    return lax.all_to_all(panel, BLK, split_axis=1, concat_axis=2, tiled=True)


def to_blocks(panel):
    return lax.all_to_all(panel, BLK, split_axis=2, concat_axis=1, tiled=True)


def dp_sum(total, sizes):
    lanes = total.shape[-1]
    for axis in DP_ORDER[:-1]:
        count = sizes[axis]
        pieces = lax.all_to_all(total.reshape(count, -1, lanes), axis, 0, 0, tiled=True)
        total = pieces.sum(axis=0)
    count = sizes[DP_ORDER[-1]]
    spread = jnp.broadcast_to(total[None], (count,) + total.shape)
    total = lax.all_to_all(spread, DP_ORDER[-1], 0, 0, tiled=True).sum(axis=0)
    for axis in reversed(DP_ORDER[:-1]):
        count = sizes[axis]
        spread = jnp.broadcast_to(total[None], (count,) + total.shape)
        total = lax.all_to_all(spread, axis, 0, 0, tiled=True).reshape(-1, lanes)
    return total


def shards(tokens, up_first, up_mix, down_mix, down_last, cotangent):
    mesh_sizes = {"core": 2, "y": 8, "zh": 4}
    flt = jnp.float32
    half = jnp.bfloat16
    row_count = tokens.shape[0]
    local_blocks = up_first.shape[0]
    width_in = up_first.shape[1]
    inputs = tokens.reshape(row_count, local_blocks, width_in)
    outgrads = cotangent.reshape(row_count, local_blocks, width_in)
    first = jnp.einsum("trk,rkc->trc", inputs, up_first, preferred_element_type=flt).astype(half)
    grad_mixed = jnp.einsum("tqk,qkc->tqc", outgrads, down_last, preferred_element_type=flt).astype(
        half
    )
    first_tok, grad_mixed_tok = to_tokens(jnp.stack([first, grad_mixed]))
    pre_tok = jnp.einsum("trc,csr->tsc", first_tok, up_mix, preferred_element_type=flt).astype(half)
    hidden_f, slope = gelu_pair(pre_tok.astype(flt))
    hidden_tok = hidden_f.astype(half)
    mixed_tok = jnp.einsum("tsc,cqs->tqc", hidden_tok, down_mix, preferred_element_type=flt).astype(
        half
    )
    grad_hidden_tok = jnp.einsum(
        "tqc,cqs->tsc", grad_mixed_tok, down_mix, preferred_element_type=flt
    ).astype(half)
    grad_pre_tok = (grad_hidden_tok.astype(flt) * slope).astype(half)
    grad_first_tok = jnp.einsum(
        "tsc,csr->trc", grad_pre_tok, up_mix, preferred_element_type=flt
    ).astype(half)
    mixed, grad_first = to_blocks(jnp.stack([mixed_tok, grad_first_tok]))
    encoded = jnp.einsum("tqc,qkc->tqk", mixed, down_last, preferred_element_type=flt).astype(half)
    grad_last = jnp.einsum("tqk,tqc->qkc", outgrads, mixed, preferred_element_type=flt)
    grad_in = jnp.einsum("trc,rkc->trk", grad_first, up_first, preferred_element_type=flt).astype(
        half
    )
    grad_firstw = jnp.einsum("trk,trc->rkc", inputs, grad_first, preferred_element_type=flt)

    both = jnp.concatenate([grad_firstw.reshape(-1, grad_firstw.shape[-1]), grad_last.reshape(-1, grad_last.shape[-1])], axis=0)
    both = dp_sum(both, mesh_sizes)
    summed_first, summed_last = jnp.split(both, 2, axis=0)
    summed_first = summed_first.reshape(grad_firstw.shape)
    summed_last = summed_last.reshape(grad_last.shape)
    return (
        encoded.reshape(row_count, local_blocks * width_in),
        grad_in.reshape(row_count, local_blocks * width_in),
        summed_first,
        summed_last,
    )


def solution(mesh):
    mesh = Mesh(mesh.devices.reshape(8, 4, 2, 3, 4), ("y", "zh", "core", "zl", "x"))
    placed = (
        P(DP, BLK),
        P(BLK, None, None),
        P(),
        P(),
        P(BLK, None, None),
        P(DP, BLK),
    )
    return jax.shard_map(
        shards,
        mesh=mesh,
        in_specs=placed,
        out_specs=(
            P(DP, BLK),
            P(DP, BLK),
            P(BLK, None, None),
            P(BLK, None, None),
        ),
        check_vma=False,
    )
```

```python
import jax
import jax.numpy as jnp
from jax import lax
from jax.sharding import PartitionSpec as P, Mesh
DP = ("y", "zh", "core")
BLK = ("zl", "x")
DP_ORDER = ("core", "y", "zh")
CHUNKS = 2

gelu_coef = 0.7978845608028654
cubic_coef = 0.044715


def gelu_pair(values):
    inner = gelu_coef * (values + cubic_coef * values * values * values)
    tangent = jnp.tanh(inner)
    result = 0.5 * values * (1.0 + tangent)
    slope = 0.5 * (1.0 + tangent) + 0.5 * values * (1.0 - tangent * tangent) * gelu_coef * (
        1.0 + 3.0 * cubic_coef * values * values
    )
    return (result, slope)


def to_tokens(panel):
    return lax.all_to_all(panel, BLK, split_axis=1, concat_axis=2, tiled=True)


def to_blocks(panel):
    return lax.all_to_all(panel, BLK, split_axis=2, concat_axis=1, tiled=True)


def dp_sum(total, sizes):
    lanes = total.shape[-1]
    for axis in DP_ORDER[:-1]:
        count = sizes[axis]
        pieces = lax.all_to_all(total.reshape(count, -1, lanes), axis, 0, 0, tiled=True)
        total = pieces.sum(axis=0)
    count = sizes[DP_ORDER[-1]]
    spread = jnp.broadcast_to(total[None], (count,) + total.shape)
    total = lax.all_to_all(spread, DP_ORDER[-1], 0, 0, tiled=True).sum(axis=0)
    for axis in reversed(DP_ORDER[:-1]):
        count = sizes[axis]
        spread = jnp.broadcast_to(total[None], (count,) + total.shape)
        total = lax.all_to_all(spread, axis, 0, 0, tiled=True).reshape(-1, lanes)
    return total


def pipeline(inputs, outgrads, up_first, up_mix, down_mix, down_last):
    flt = jnp.float32
    half = jnp.bfloat16
    first = jnp.einsum("trk,rkc->trc", inputs, up_first, preferred_element_type=flt).astype(half)
    grad_mixed = jnp.einsum("tqk,qkc->tqc", outgrads, down_last, preferred_element_type=flt).astype(
        half
    )
    first_tok, grad_mixed_tok = to_tokens(jnp.stack([first, grad_mixed]))
    pre_tok = jnp.einsum("trc,csr->tsc", first_tok, up_mix, preferred_element_type=flt).astype(half)
    hidden_f, slope = gelu_pair(pre_tok.astype(flt))
    hidden_tok = hidden_f.astype(half)
    mixed_tok = jnp.einsum("tsc,cqs->tqc", hidden_tok, down_mix, preferred_element_type=flt).astype(
        half
    )
    grad_hidden_tok = jnp.einsum(
        "tqc,cqs->tsc", grad_mixed_tok, down_mix, preferred_element_type=flt
    ).astype(half)
    grad_pre_tok = (grad_hidden_tok.astype(flt) * slope).astype(half)
    grad_first_tok = jnp.einsum(
        "tsc,csr->trc", grad_pre_tok, up_mix, preferred_element_type=flt
    ).astype(half)
    mixed, grad_first = to_blocks(jnp.stack([mixed_tok, grad_first_tok]))
    encoded = jnp.einsum("tqc,qkc->tqk", mixed, down_last, preferred_element_type=flt).astype(half)
    grad_last = jnp.einsum("tqk,tqc->qkc", outgrads, mixed, preferred_element_type=flt)
    grad_in = jnp.einsum("trc,rkc->trk", grad_first, up_first, preferred_element_type=flt).astype(
        half
    )
    grad_firstw = jnp.einsum("trk,trc->rkc", inputs, grad_first, preferred_element_type=flt)

    return encoded, grad_in, grad_firstw, grad_last


def shards(tokens, up_first, up_mix, down_mix, down_last, cotangent):
    mesh_sizes = {"core": 2, "y": 8, "zh": 4}
    flt = jnp.float32
    half = jnp.bfloat16
    row_count = tokens.shape[0]
    local_blocks = up_first.shape[0]
    width_in = up_first.shape[1]
    inputs = tokens.reshape(row_count, local_blocks, width_in)
    outgrads = cotangent.reshape(row_count, local_blocks, width_in)
    pieces = [
        pipeline(inputs[rows], outgrads[rows], up_first, up_mix, down_mix, down_last)
        for rows in (slice(i * row_count // CHUNKS, (i + 1) * row_count // CHUNKS) for i in range(CHUNKS))
    ]
    encoded = jnp.concatenate([piece[0] for piece in pieces], axis=0)
    grad_in = jnp.concatenate([piece[1] for piece in pieces], axis=0)
    grad_firstw = sum(piece[2] for piece in pieces[1:]) + pieces[0][2]
    grad_last = sum(piece[3] for piece in pieces[1:]) + pieces[0][3]
    both = jnp.concatenate([grad_firstw.reshape(-1, grad_firstw.shape[-1]), grad_last.reshape(-1, grad_last.shape[-1])], axis=0)
    both = dp_sum(both, mesh_sizes)
    summed_first, summed_last = jnp.split(both, 2, axis=0)
    summed_first = summed_first.reshape(grad_firstw.shape)
    summed_last = summed_last.reshape(grad_last.shape)
    return (
        encoded.reshape(row_count, local_blocks * width_in),
        grad_in.reshape(row_count, local_blocks * width_in),
        summed_first,
        summed_last,
    )


def solution(mesh):
    mesh = Mesh(mesh.devices.reshape(8, 4, 2, 3, 4), ("y", "zh", "core", "zl", "x"))
    placed = (
        P(DP, BLK),
        P(BLK, None, None),
        P(),
        P(),
        P(BLK, None, None),
        P(DP, BLK),
    )
    return jax.shard_map(
        shards,
        mesh=mesh,
        in_specs=placed,
        out_specs=(
            P(DP, BLK),
            P(DP, BLK),
            P(BLK, None, None),
            P(BLK, None, None),
        ),
        check_vma=False,
    )
```

```python
import jax
import jax.numpy as jnp
from jax import lax
from jax.sharding import PartitionSpec as P, Mesh
DP = ("y", "zh", "core")
BLK = ("zl", "x")
DP_ORDER = ("core", "y", "zh")

gelu_coef = 0.7978845608028654
cubic_coef = 0.044715


def gelu_pair(values):
    inner = gelu_coef * (values + cubic_coef * values * values * values)
    tangent = jnp.tanh(inner)
    result = 0.5 * values * (1.0 + tangent)
    slope = 0.5 * (1.0 + tangent) + 0.5 * values * (1.0 - tangent * tangent) * gelu_coef * (
        1.0 + 3.0 * cubic_coef * values * values
    )
    return (result, slope)


def to_tokens(panel):
    return lax.all_to_all(panel, BLK, split_axis=1, concat_axis=2, tiled=True)


def to_blocks(panel):
    return lax.all_to_all(panel, BLK, split_axis=2, concat_axis=1, tiled=True)


def dp_sum(total, sizes):
    lanes = total.shape[-1]
    near = ("y", "core")
    count = sizes["y"] * sizes["core"]
    pieces = lax.all_to_all(total.reshape(count, -1, lanes), near, 0, 0, tiled=True)
    total = pieces.sum(axis=0)
    far = sizes["zh"]
    spread = jnp.broadcast_to(total[None], (far,) + total.shape)
    total = lax.all_to_all(spread, "zh", 0, 0, tiled=True).sum(axis=0)
    spread = jnp.broadcast_to(total[None], (count,) + total.shape)
    return lax.all_to_all(spread, near, 0, 0, tiled=True).reshape(-1, lanes)


def shards(tokens, up_first, up_mix, down_mix, down_last, cotangent):
    mesh_sizes = {"core": 2, "y": 8, "zh": 4}
    flt = jnp.float32
    half = jnp.bfloat16
    row_count = tokens.shape[0]
    local_blocks = up_first.shape[0]
    width_in = up_first.shape[1]
    inputs = tokens.reshape(row_count, local_blocks, width_in)
    outgrads = cotangent.reshape(row_count, local_blocks, width_in)
    first = jnp.einsum("trk,rkc->trc", inputs, up_first, preferred_element_type=flt).astype(half)
    grad_mixed = jnp.einsum("tqk,qkc->tqc", outgrads, down_last, preferred_element_type=flt).astype(
        half
    )
    first_tok, grad_mixed_tok = to_tokens(jnp.stack([first, grad_mixed]))
    pre_tok = jnp.einsum("trc,csr->tsc", first_tok, up_mix, preferred_element_type=flt).astype(half)
    hidden_f, slope = gelu_pair(pre_tok.astype(flt))
    hidden_tok = hidden_f.astype(half)
    mixed_tok = jnp.einsum("tsc,cqs->tqc", hidden_tok, down_mix, preferred_element_type=flt).astype(
        half
    )
    grad_hidden_tok = jnp.einsum(
        "tqc,cqs->tsc", grad_mixed_tok, down_mix, preferred_element_type=flt
    ).astype(half)
    grad_pre_tok = (grad_hidden_tok.astype(flt) * slope).astype(half)
    grad_first_tok = jnp.einsum(
        "tsc,csr->trc", grad_pre_tok, up_mix, preferred_element_type=flt
    ).astype(half)
    mixed, grad_first = to_blocks(jnp.stack([mixed_tok, grad_first_tok]))
    encoded = jnp.einsum("tqc,qkc->tqk", mixed, down_last, preferred_element_type=flt).astype(half)
    grad_last = jnp.einsum("tqk,tqc->qkc", outgrads, mixed, preferred_element_type=flt)
    grad_in = jnp.einsum("trc,rkc->trk", grad_first, up_first, preferred_element_type=flt).astype(
        half
    )
    grad_firstw = jnp.einsum("trk,trc->rkc", inputs, grad_first, preferred_element_type=flt)

    both = jnp.concatenate([grad_firstw.reshape(-1, grad_firstw.shape[-1]), grad_last.reshape(-1, grad_last.shape[-1])], axis=0)
    both = dp_sum(both, mesh_sizes)
    summed_first, summed_last = jnp.split(both, 2, axis=0)
    summed_first = summed_first.reshape(grad_firstw.shape)
    summed_last = summed_last.reshape(grad_last.shape)
    return (
        encoded.reshape(row_count, local_blocks * width_in),
        grad_in.reshape(row_count, local_blocks * width_in),
        summed_first,
        summed_last,
    )


def solution(mesh):
    mesh = Mesh(mesh.devices.reshape(8, 4, 2, 3, 4), ("y", "zh", "core", "zl", "x"))
    placed = (
        P(DP, BLK),
        P(BLK, None, None),
        P(),
        P(),
        P(BLK, None, None),
        P(DP, BLK),
    )
    return jax.shard_map(
        shards,
        mesh=mesh,
        in_specs=placed,
        out_specs=(
            P(DP, BLK),
            P(DP, BLK),
            P(BLK, None, None),
            P(BLK, None, None),
        ),
        check_vma=False,
    )
```

```python
import jax
import jax.numpy as jnp
from jax import lax
from jax.sharding import PartitionSpec as P, Mesh
DP = ("y", "zh", "core")
BLK = ("zl", "x")
DP_ORDER = ("core", "y", "zh")
ZL, XS = 3, 4

gelu_coef = 0.7978845608028654
cubic_coef = 0.044715


def gelu_pair(values):
    inner = gelu_coef * (values + cubic_coef * values * values * values)
    tangent = jnp.tanh(inner)
    result = 0.5 * values * (1.0 + tangent)
    slope = 0.5 * (1.0 + tangent) + 0.5 * values * (1.0 - tangent * tangent) * gelu_coef * (
        1.0 + 3.0 * cubic_coef * values * values
    )
    return (result, slope)


def to_mixing(panel):
    pair, rows, blocks, hidden = panel.shape
    part = hidden // XS
    panel = panel.reshape(pair, ZL, rows // ZL, blocks, XS, part).transpose(0, 1, 4, 2, 3, 5)
    panel = panel.reshape(pair, ZL * XS, rows // ZL, blocks, part)
    panel = lax.all_to_all(panel, BLK, split_axis=1, concat_axis=3, tiled=True)
    return panel.reshape(pair, rows // ZL, blocks * ZL * XS, part).transpose(0, 3, 1, 2)


def from_mixing(panel):
    pair, part, rows, width = panel.shape
    blocks = width // (ZL * XS)
    panel = panel.reshape(pair, part, rows, ZL * XS, blocks).transpose(0, 3, 1, 2, 4)
    panel = lax.all_to_all(panel, BLK, split_axis=1, concat_axis=1, tiled=True)
    panel = panel.reshape(pair, ZL, XS, part, rows, blocks).transpose(0, 1, 4, 5, 2, 3)
    return panel.reshape(pair, ZL * rows, blocks, XS * part)


def dp_sum(total, sizes):
    lanes = total.shape[-1]
    for axis in DP_ORDER[:-1]:
        count = sizes[axis]
        pieces = lax.all_to_all(total.reshape(count, -1, lanes), axis, 0, 0, tiled=True)
        total = pieces.sum(axis=0)
    count = sizes[DP_ORDER[-1]]
    spread = jnp.broadcast_to(total[None], (count,) + total.shape)
    total = lax.all_to_all(spread, DP_ORDER[-1], 0, 0, tiled=True).sum(axis=0)
    for axis in reversed(DP_ORDER[:-1]):
        count = sizes[axis]
        spread = jnp.broadcast_to(total[None], (count,) + total.shape)
        total = lax.all_to_all(spread, axis, 0, 0, tiled=True).reshape(-1, lanes)
    return total


def shards(tokens, up_first, up_mix, down_mix, down_last, cotangent):
    mesh_sizes = {"core": 2, "y": 8, "zh": 4}
    flt = jnp.float32
    half = jnp.bfloat16
    row_count = tokens.shape[0]
    local_blocks = up_first.shape[0]
    width_in = up_first.shape[1]
    inputs = tokens.reshape(row_count, local_blocks, width_in)
    outgrads = cotangent.reshape(row_count, local_blocks, width_in)
    first = jnp.einsum("trk,rkc->trc", inputs, up_first, preferred_element_type=flt).astype(half)
    grad_mixed = jnp.einsum("tqk,qkc->tqc", outgrads, down_last, preferred_element_type=flt).astype(
        half
    )
    part = up_mix.shape[0] // XS
    column = lax.axis_index("x") * part
    up_mix_l = lax.dynamic_slice_in_dim(up_mix, column, part, axis=0)
    down_mix_l = lax.dynamic_slice_in_dim(down_mix, column, part, axis=0)
    first_m, grad_mixed_m = to_mixing(jnp.stack([first, grad_mixed]))
    pre_m = jnp.einsum("ctr,csr->cts", first_m, up_mix_l, preferred_element_type=flt).astype(half)
    hidden_f, slope = gelu_pair(pre_m.astype(flt))
    hidden_m = hidden_f.astype(half)
    mixed_m = jnp.einsum("cts,cqs->ctq", hidden_m, down_mix_l, preferred_element_type=flt).astype(
        half
    )
    grad_hidden_m = jnp.einsum(
        "ctq,cqs->cts", grad_mixed_m, down_mix_l, preferred_element_type=flt
    ).astype(half)
    grad_pre_m = (grad_hidden_m.astype(flt) * slope).astype(half)
    grad_first_m = jnp.einsum(
        "cts,csr->ctr", grad_pre_m, up_mix_l, preferred_element_type=flt
    ).astype(half)
    mixed, grad_first = from_mixing(jnp.stack([mixed_m, grad_first_m]))
    encoded = jnp.einsum("tqc,qkc->tqk", mixed, down_last, preferred_element_type=flt).astype(half)
    grad_last = jnp.einsum("tqk,tqc->qkc", outgrads, mixed, preferred_element_type=flt)
    grad_in = jnp.einsum("trc,rkc->trk", grad_first, up_first, preferred_element_type=flt).astype(
        half
    )
    grad_firstw = jnp.einsum("trk,trc->rkc", inputs, grad_first, preferred_element_type=flt)

    both = jnp.concatenate([grad_firstw.reshape(-1, grad_firstw.shape[-1]), grad_last.reshape(-1, grad_last.shape[-1])], axis=0)
    both = dp_sum(both, mesh_sizes)
    summed_first, summed_last = jnp.split(both, 2, axis=0)
    summed_first = summed_first.reshape(grad_firstw.shape)
    summed_last = summed_last.reshape(grad_last.shape)
    return (
        encoded.reshape(row_count, local_blocks * width_in),
        grad_in.reshape(row_count, local_blocks * width_in),
        summed_first,
        summed_last,
    )


def solution(mesh):
    mesh = Mesh(mesh.devices.reshape(8, 4, 2, 3, 4), ("y", "zh", "core", "zl", "x"))
    placed = (
        P(DP, BLK),
        P(BLK, None, None),
        P(),
        P(),
        P(BLK, None, None),
        P(DP, BLK),
    )
    return jax.shard_map(
        shards,
        mesh=mesh,
        in_specs=placed,
        out_specs=(
            P(DP, BLK),
            P(DP, BLK),
            P(BLK, None, None),
            P(BLK, None, None),
        ),
        check_vma=False,
    )
```

```python
import jax
import jax.numpy as jnp
from jax import lax
from jax.sharding import PartitionSpec as P, Mesh
DP = ("y", "zh", "core")
BLK = ("zl", "x")
DP_ORDER = ("core", "y", "zh")
GROUPS, HALVES = 12, 2

gelu_coef = 0.7978845608028654
cubic_coef = 0.044715


def gelu_pair(values):
    inner = gelu_coef * (values + cubic_coef * values * values * values)
    tangent = jnp.tanh(inner)
    result = 0.5 * values * (1.0 + tangent)
    slope = 0.5 * (1.0 + tangent) + 0.5 * values * (1.0 - tangent * tangent) * gelu_coef * (
        1.0 + 3.0 * cubic_coef * values * values
    )
    return (result, slope)


def to_tokens(panel):
    pair, rows, blocks, hidden = panel.shape
    part = hidden // HALVES
    groups = GROUPS // HALVES
    panel = panel.reshape(pair, groups, rows // groups, blocks, HALVES, part).transpose(0, 1, 4, 2, 3, 5)
    panel = panel.reshape(pair, GROUPS, rows // groups, blocks, part)
    panel = lax.all_to_all(panel, BLK, split_axis=1, concat_axis=3, tiled=True)
    return panel.reshape(pair, rows // groups, blocks * GROUPS, part)


def to_blocks(panel):
    pair, rows, width, part = panel.shape
    blocks = width // GROUPS
    groups = GROUPS // HALVES
    panel = panel.reshape(pair, rows, GROUPS, blocks, part).transpose(0, 2, 1, 3, 4)
    panel = lax.all_to_all(panel, BLK, split_axis=1, concat_axis=1, tiled=True)
    panel = panel.reshape(pair, groups, HALVES, rows, blocks, part).transpose(0, 1, 3, 4, 2, 5)
    return panel.reshape(pair, groups * rows, blocks, HALVES * part)


def dp_sum(total, sizes):
    lanes = total.shape[-1]
    for axis in DP_ORDER[:-1]:
        count = sizes[axis]
        pieces = lax.all_to_all(total.reshape(count, -1, lanes), axis, 0, 0, tiled=True)
        total = pieces.sum(axis=0)
    count = sizes[DP_ORDER[-1]]
    spread = jnp.broadcast_to(total[None], (count,) + total.shape)
    total = lax.all_to_all(spread, DP_ORDER[-1], 0, 0, tiled=True).sum(axis=0)
    for axis in reversed(DP_ORDER[:-1]):
        count = sizes[axis]
        spread = jnp.broadcast_to(total[None], (count,) + total.shape)
        total = lax.all_to_all(spread, axis, 0, 0, tiled=True).reshape(-1, lanes)
    return total


def shards(tokens, up_first, up_mix, down_mix, down_last, cotangent):
    mesh_sizes = {"core": 2, "y": 8, "zh": 4}
    flt = jnp.float32
    half = jnp.bfloat16
    row_count = tokens.shape[0]
    local_blocks = up_first.shape[0]
    width_in = up_first.shape[1]
    inputs = tokens.reshape(row_count, local_blocks, width_in)
    outgrads = cotangent.reshape(row_count, local_blocks, width_in)
    first = jnp.einsum("trk,rkc->trc", inputs, up_first, preferred_element_type=flt).astype(half)
    grad_mixed = jnp.einsum("tqk,qkc->tqc", outgrads, down_last, preferred_element_type=flt).astype(
        half
    )
    part = up_mix.shape[0] // HALVES
    column = lax.rem(lax.axis_index("x"), HALVES) * part
    up_mix = lax.dynamic_slice_in_dim(up_mix, column, part, axis=0)
    down_mix = lax.dynamic_slice_in_dim(down_mix, column, part, axis=0)
    first_tok, grad_mixed_tok = to_tokens(jnp.stack([first, grad_mixed]))
    pre_tok = jnp.einsum("trc,csr->tsc", first_tok, up_mix, preferred_element_type=flt).astype(half)
    hidden_f, slope = gelu_pair(pre_tok.astype(flt))
    hidden_tok = hidden_f.astype(half)
    mixed_tok = jnp.einsum("tsc,cqs->tqc", hidden_tok, down_mix, preferred_element_type=flt).astype(
        half
    )
    grad_hidden_tok = jnp.einsum(
        "tqc,cqs->tsc", grad_mixed_tok, down_mix, preferred_element_type=flt
    ).astype(half)
    grad_pre_tok = (grad_hidden_tok.astype(flt) * slope).astype(half)
    grad_first_tok = jnp.einsum(
        "tsc,csr->trc", grad_pre_tok, up_mix, preferred_element_type=flt
    ).astype(half)
    mixed, grad_first = to_blocks(jnp.stack([mixed_tok, grad_first_tok]))
    encoded = jnp.einsum("tqc,qkc->tqk", mixed, down_last, preferred_element_type=flt).astype(half)
    grad_last = jnp.einsum("tqk,tqc->qkc", outgrads, mixed, preferred_element_type=flt)
    grad_in = jnp.einsum("trc,rkc->trk", grad_first, up_first, preferred_element_type=flt).astype(
        half
    )
    grad_firstw = jnp.einsum("trk,trc->rkc", inputs, grad_first, preferred_element_type=flt)

    both = jnp.concatenate([grad_firstw.reshape(-1, grad_firstw.shape[-1]), grad_last.reshape(-1, grad_last.shape[-1])], axis=0)
    both = dp_sum(both, mesh_sizes)
    summed_first, summed_last = jnp.split(both, 2, axis=0)
    summed_first = summed_first.reshape(grad_firstw.shape)
    summed_last = summed_last.reshape(grad_last.shape)
    return (
        encoded.reshape(row_count, local_blocks * width_in),
        grad_in.reshape(row_count, local_blocks * width_in),
        summed_first,
        summed_last,
    )


def solution(mesh):
    mesh = Mesh(mesh.devices.reshape(8, 4, 2, 3, 4), ("y", "zh", "core", "zl", "x"))
    placed = (
        P(DP, BLK),
        P(BLK, None, None),
        P(),
        P(),
        P(BLK, None, None),
        P(DP, BLK),
    )
    return jax.shard_map(
        shards,
        mesh=mesh,
        in_specs=placed,
        out_specs=(
            P(DP, BLK),
            P(DP, BLK),
            P(BLK, None, None),
            P(BLK, None, None),
        ),
        check_vma=False,
    )
```
